256 devices in a mesh: dp: 8 (over x, core), expert: 32 (over y, z).
Axes of the slice: x: 4, y: 4, z: 8, core: 2. Of those that a mesh axis runs over, the one named last changes fastest.
Arguments:
- tokens: bfloat16 [32768, 2048], P(('dp', 'expert')), may hold values from -6 to 6
- cotangent: bfloat16 [32768, 2048], P(('dp', 'expert')), may hold values from -6 to 6
- router_logits: float32 [32768, 2], P(('dp', 'expert')), may hold values from -5 to 5
- expert_ids: int32 [32768, 2], P(('dp', 'expert')), may hold values from 0 to 31, all different within a row; in each aligned block of 128 rows (0 to 127, 128 to 255, ...) at most 14 rows name the same one
- w_in: bfloat16 [32, 2048, 1536], P('expert', 'dp'), may hold values from -0.125 to 0.125
- w_out: bfloat16 [32, 768, 2048], P('expert', 'dp'), may hold values from -0.21875 to 0.21875
Outputs:
- mixed: bfloat16 [32768, 2048], P(('dp', 'expert'))
- d_tokens: bfloat16 [32768, 2048], P(('dp', 'expert'))
- d_logits: float32 [32768, 2], P(('dp', 'expert'))
- grad_in: float32 [32, 2048, 1536], P('expert', 'dp')
- grad_out: float32 [32, 768, 2048], P('expert', 'dp')
The draws below stay inside these ranges and needn't reach their ends.
Inputs may be any that keep to these rules, and one draw needn't show every extreme that they name: `expert_ids`: the 2 experts of a token differ; among the tokens of one device, no expert is chosen more than 14 times, and some expert is chosen exactly 14 times by some device.
All inputs are finite; a program needn't handle non-finite values.
Results may differ from the reference program's by a relative error of at most 0.015.
Values may be sent and summed in bfloat16 or wider, within the bound.
No kernel may reach another device: no remote copies, remote signals or barrier semaphores. Data moves between devices by JAX's collectives and lax.ppermute only.
A program may use at most 128 MiB of HBM per device.

```python
import math
import jax
import jax.numpy as jnp
import numpy as np
from jax import lax

D = 2048
FF = 768
TOP = 2
TOK_DEV = 128
EXPERTS = 32
CAP = 14
TOKENS = 32768
N_DP = 8
N_EXPERT = 32
DEVICES = 256


def block_levels(own_key, shape, split, least, top_value):
    factor_of, own = 1.0, jax.random.fold_in(own_key, 6)
    for axis_at, parts in split:
        steps = jnp.exp(jax.random.uniform(jax.random.fold_in(own, axis_at), (parts,), jnp.float32, least / len(split), top_value / len(split)))
        factor_of = factor_of * jnp.repeat(steps, shape[axis_at] // parts).reshape([-1 if axis == axis_at else 1 for axis in range(len(shape))])
    return factor_of


def assign_block(stream_key, own, number, rows, count, top, most, lean):
    ranking = jax.random.permutation(stream_key, count)
    heavy_load, usual = shares(count, rows * top, most, lean, True), shares(count, rows * top, most, lean, False)
    places = jnp.arange(count)

    def named(lengths, rotation):
        used = int((lengths > 0).sum())
        fixed = max(1, used // 4)
        shifted = fixed + (places - fixed + rotation * (used - fixed)) % max(1, count - fixed)
        return jnp.zeros((count,), jnp.int32).at[ranking[jnp.where(places < fixed, places, shifted)]].set(jnp.asarray(lengths, jnp.int32))

    lengths = jnp.where(number % 4 == 0, named(heavy_load, number // 4), named(usual, number - number // 4 - 1))
    mixed = jax.random.permutation(jax.random.fold_in(own, 3), count)
    giver, receiver = mixed[0:count // 2 * 2:2], mixed[1:count // 2 * 2:2]
    slack = jnp.minimum(lengths[giver] - 1, most - lengths[receiver]) // 2
    slack = jnp.where((giver == ranking[0]) | (receiver == ranking[0]) | (lengths[receiver] == 0), 0, jnp.maximum(slack, 0))
    shifted = jax.random.randint(jax.random.fold_in(own, 4), (count // 2,), 0, 1 << 20) % (slack + 1)
    lengths = lengths.at[giver].add(-shifted).at[receiver].add(shifted)
    labels = jnp.searchsorted(jnp.cumsum(lengths), jnp.arange(rows * top), side="right").astype(jnp.int32)
    grid = labels.reshape(top, rows).T
    grid = grid[jax.random.permutation(jax.random.fold_in(own, 1), rows)]
    rotation = jax.random.randint(jax.random.fold_in(own, 2), (rows, 1), 0, top)
    return jnp.take_along_axis(grid, (jnp.arange(top)[None, :] + rotation) % top, axis=1)


def shares(count, total, most, slope, full):
    portions = [(1 << 20) // math.isqrt(rank ** slope) + 1 for rank in range(1, count + 1)]
    largest = most if full else min(most, max(-(-total // count), total * portions[0] // sum(portions)))
    least = 1 if total - largest >= count - 1 else 0
    counts, spare = [largest] + [least] * (count - 1), total - largest - least * (count - 1)
    while spare > 0:
        candidates = [i for i in range(1, count) if counts[i] < largest] or [i for i in range(1, count) if counts[i] < most]
        whole, budget = sum([portions[i] for i in candidates]), spare
        for i in candidates:
            extra = min(most - counts[i], max(1, budget * portions[i] // whole), spare)
            counts[i] = counts[i] + extra
            spare = spare - extra
    return np.array(counts)


def centred(stream_key, dims, width, most, pieces=(), held_as=jnp.bfloat16):
    entries = jax.random.normal(stream_key, dims, jnp.float32) * width
    if len(pieces) > 0:
        entries = block_levels(stream_key, dims, pieces, -0.22, 0.18) * entries
    return jnp.clip(entries, min=-most, max=most).astype(held_as)


def setup_inputs(seed: int = 0) -> dict:
    keys = jax.random.split(jax.random.key(seed), 7)
    tokens = centred(keys[0], (TOKENS, D), 1.0, 6.0, ((0, 256),))
    cotangent = centred(keys[1], (TOKENS, D), 1.0, 6.0, ((0, 256),))
    router_logits = centred(keys[2], (TOKENS, TOP), 1.0, 5.0, ((0, 256),), jnp.float32)
    expert_ids_keys = jax.random.split(jax.random.fold_in(keys[3], 1), TOKENS // TOK_DEV)
    expert_ids_turns = jax.random.permutation(jax.random.fold_in(keys[3], 3), TOKENS // TOK_DEV)
    expert_ids = jax.vmap(lambda own, number: assign_block(jax.random.fold_in(keys[3], 2), own, number, TOK_DEV, EXPERTS, TOP, CAP, 2))(expert_ids_keys, expert_ids_turns).reshape((TOKENS, TOP))
    w_in = centred(keys[4], (EXPERTS, D, 2 * FF), D ** -0.5, 0.125, ((0, 32), (1, 8)))
    w_out = centred(keys[5], (EXPERTS, FF, D), FF ** -0.5, 0.21875, ((0, 32), (1, 8)))
    return {"tokens": tokens, "cotangent": cotangent, "router_logits": router_logits, "expert_ids": expert_ids, "w_in": w_in, "w_out": w_out}


def positions(expert_ids):
    flat = expert_ids.reshape(DEVICES, TOK_DEV * TOP)
    onehot = (flat[:, :, None] == jnp.arange(EXPERTS, dtype=jnp.int32)[None, None, :]).astype(jnp.int32)
    before = jnp.cumsum(onehot, axis=1) - onehot
    return jnp.sum(before * onehot, axis=-1).reshape(TOKENS, TOP).astype(jnp.int32)


def reference(tokens, cotangent, router_logits, expert_ids, w_in, w_out):
    f32 = jnp.float32
    position = positions(expert_ids)
    token_index = jnp.broadcast_to(jnp.arange(TOKENS, dtype=jnp.int32)[:, None], (TOKENS, TOP))
    block = token_index // TOK_DEV
    pick = jnp.arange(TOKENS * TOP, dtype=jnp.int32).reshape(TOKENS, TOP)
    table = jnp.full((EXPERTS, DEVICES, CAP), TOKENS * TOP, jnp.int32)
    table = table.at[expert_ids, block, position].set(pick)
    diffs = router_logits[:, None, :] - router_logits[:, :, None]
    gates = 1.0 / jnp.sum(jnp.exp(diffs), axis=-1)
    x_pad = jnp.concatenate([tokens, jnp.zeros((1, D), jnp.bfloat16)], axis=0)
    dy_pad = jnp.concatenate([cotangent, jnp.zeros((1, D), jnp.bfloat16)], axis=0)
    g_flat = jnp.concatenate([gates.reshape(-1), jnp.zeros((1,), f32)], axis=0)

    def per_expert(carry, inputs):
        mixed_acc, dx_acc, dgate_acc = carry
        slots, win, wout = inputs
        slots = slots.reshape(N_DP, N_EXPERT * CAP)
        tok = jnp.where(slots < TOKENS * TOP, slots // TOP, TOKENS).astype(jnp.int32)
        x = x_pad[tok]
        g = g_flat[slots]
        dyr = dy_pad[tok].astype(f32)
        joined = jnp.einsum('prd,df->prf', x.astype(f32), win.astype(f32))
        a = joined[..., :FF]
        u = joined[..., FF:]
        s = 1.0 / (1.0 + jnp.exp(-a))
        silu = a * s
        hidden = (silu * u).astype(jnp.bfloat16)
        result = jnp.einsum('prf,fd->prd', hidden.astype(f32), wout.astype(f32)).astype(jnp.bfloat16)
        d_result = (g[..., None] * dyr).astype(jnp.bfloat16)
        d_hidden = jnp.einsum('prd,fd->prf', d_result.astype(f32), wout.astype(f32))
        d_joined = jnp.concatenate([d_hidden * u * s * (1.0 + a * (1.0 - s)), d_hidden * silu], axis=-1).astype(jnp.bfloat16)
        d_pick = jnp.einsum('prf,df->prd', d_joined.astype(f32), win.astype(f32)).astype(jnp.bfloat16)
        part_out = jnp.einsum('prf,prd->pfd', hidden.astype(f32), d_result.astype(f32)).astype(jnp.bfloat16)
        part_in = jnp.einsum('prd,prf->pdf', x.astype(f32), d_joined.astype(f32)).astype(jnp.bfloat16)
        part_out = lax.optimization_barrier(part_out)
        part_in = lax.optimization_barrier(part_in)
        grad_out_e = jnp.sum(part_out.astype(f32), axis=0)
        grad_in_e = jnp.sum(part_in.astype(f32), axis=0)
        result32 = result.astype(f32)
        dgate = jnp.sum(dyr * result32, axis=-1)
        flat_tok = tok.reshape(-1)
        mixed_acc = mixed_acc.at[flat_tok].add((g[..., None] * result32).reshape(-1, D), mode="drop")
        dx_acc = dx_acc.at[flat_tok].add(d_pick.astype(f32).reshape(-1, D), mode="drop")
        dgate_acc = dgate_acc.at[slots.reshape(-1)].set(dgate.reshape(-1), mode="drop")
        return (mixed_acc, dx_acc, dgate_acc), (grad_in_e, grad_out_e)

    init = (jnp.zeros((TOKENS, D), f32), jnp.zeros((TOKENS, D), f32), jnp.zeros((TOKENS * TOP,), f32))
    (mixed_acc, dx_acc, dgate_acc), (grad_in, grad_out) = lax.scan(per_expert, init, (table, w_in, w_out))
    dgate = dgate_acc.reshape(TOKENS, TOP)
    d_logits = gates * (dgate - jnp.sum(gates * dgate, axis=-1, keepdims=True))
    return mixed_acc.astype(jnp.bfloat16), dx_acc.astype(jnp.bfloat16), d_logits, grad_in, grad_out
```

```python
import jax
import jax.numpy as jnp
from jax import lax
from jax.sharding import PartitionSpec as P


def contract_rows(left, right):
    return lax.dot_general(
        left, right, (((0,), (0,)), ((), ())), preferred_element_type=jnp.float32
    )


def contract_cols(left, right):
    return lax.dot_general(
        left, right, (((1,), (1,)), ((), ())), preferred_element_type=jnp.float32
    )


def local(tokens, cotangent, router_logits, expert_ids, w_in, w_out):
    f32 = jnp.float32
    bf16 = jnp.bfloat16
    tok_rows, width = tokens.shape
    top = expert_ids.shape[1]
    experts = lax.axis_size("expert")
    capacity = 7 * tok_rows * top // (4 * experts)
    gathered_in, gathered_out = (
        lax.all_gather(w_in, "dp", axis=1, tiled=True),
        lax.all_gather(w_out, "dp", axis=1, tiled=True),
    )
    in_full = gathered_in[0]
    out_full = gathered_out[0]
    ff_units = in_full.shape[1] // 2
    flat_ids = expert_ids.reshape(-1)
    onehot = (flat_ids[:, None] == jnp.arange(experts, dtype=jnp.int32)[None, :]).astype(jnp.int32)
    before = jnp.cumsum(onehot, axis=0) - onehot
    position = jnp.sum(before * onehot, axis=1)
    slot_flat = flat_ids * capacity + position
    select = (
        jnp.arange(experts * capacity, dtype=jnp.int32)[:, None] == slot_flat[None, :]
    ).astype(bf16)
    diffs = router_logits[:, None, :] - router_logits[:, :, None]
    gates = 1.0 / jnp.sum(jnp.exp(diffs), axis=-1)
    upstream = cotangent.astype(f32)
    repeated = jnp.repeat(tokens, top, axis=0)
    d_picks = (gates[:, :, None] * upstream[:, None, :]).astype(bf16).reshape(-1, width)
    sendable = jnp.concatenate([repeated, d_picks], axis=1)
    outgoing = jnp.dot(select, sendable, preferred_element_type=f32).astype(bf16)
    arrived = lax.all_to_all(
        outgoing.reshape(experts, capacity, 2 * width), "expert", split_axis=0, concat_axis=0, tiled=True
    ).reshape(-1, 2 * width)
    piece = arrived[:, :width]
    d_arrived = arrived[:, width:]
    joined = jnp.dot(piece, in_full, preferred_element_type=f32)
    gate_part = joined[:, :ff_units]
    up_part = joined[:, ff_units:]
    sigma = 1.0 / (1.0 + jnp.exp(-gate_part))
    silu = gate_part * sigma
    hidden = (silu * up_part).astype(bf16)
    results = jnp.dot(hidden, out_full, preferred_element_type=f32).astype(bf16)
    d_hidden = contract_cols(d_arrived, out_full)
    grad_down = contract_rows(hidden, d_arrived)
    d_joined = jnp.concatenate(
        [d_hidden * up_part * sigma * (1.0 + gate_part * (1.0 - sigma)), d_hidden * silu], axis=1
    ).astype(bf16)
    grad_up = contract_rows(piece, d_joined)
    up_share, down_share = (
        lax.psum_scatter(grad_up.astype(bf16), "dp", scatter_dimension=0, tiled=True).astype(f32),
        lax.psum_scatter(grad_down.astype(bf16), "dp", scatter_dimension=0, tiled=True).astype(f32),
    )
    d_rows = contract_cols(d_joined, in_full).astype(bf16)
    back = jnp.concatenate([results, d_rows], axis=1)
    returned = lax.all_to_all(
        back.reshape(experts, capacity, 2 * width), "expert", split_axis=0, concat_axis=0, tiled=True
    ).reshape(-1, 2 * width)
    picked_both = contract_rows(select, returned).reshape(tok_rows, top, 2 * width)
    picked = picked_both[:, :, :width]
    d_picked = picked_both[:, :, width:]
    mixed = jnp.einsum("tk,tkd->td", gates, picked).astype(bf16)
    d_gate = jnp.einsum("td,tkd->tk", upstream, picked)
    d_logits = gates * (d_gate - jnp.sum(gates * d_gate, axis=-1, keepdims=True))
    d_tokens = jnp.sum(d_picked, axis=1).astype(bf16)
    return (mixed, d_tokens, d_logits, up_share[None], down_share[None])


def solution(mesh):
    placed = (
        P(("dp", "expert"), None),
        P(("dp", "expert"), None),
        P(("dp", "expert"), None),
        P(("dp", "expert"), None),
        P("expert", "dp", None),
        P("expert", "dp", None),
    )
    return jax.shard_map(
        local,
        mesh=mesh,
        in_specs=placed,
        out_specs=(
            P(("dp", "expert"), None),
            P(("dp", "expert"), None),
            P(("dp", "expert"), None),
            P("expert", "dp", None),
            P("expert", "dp", None),
        ),
        check_vma=False,
    )
```

```python
import jax
import jax.numpy as jnp
from jax import lax
from jax.sharding import PartitionSpec as P


def contract_rows(left, right):
    return lax.dot_general(
        left, right, (((0,), (0,)), ((), ())), preferred_element_type=jnp.float32
    )


def contract_cols(left, right):
    return lax.dot_general(
        left, right, (((1,), (1,)), ((), ())), preferred_element_type=jnp.float32
    )


def local(tokens, cotangent, router_logits, expert_ids, w_in, w_out):
    f32 = jnp.float32
    bf16 = jnp.bfloat16
    tok_rows, width = tokens.shape
    top = expert_ids.shape[1]
    experts = lax.axis_size("expert")
    capacity = 7 * tok_rows * top // (4 * experts)
    gathered_in, gathered_out = (
        lax.all_gather(w_in, "dp", axis=1, tiled=True),
        lax.all_gather(w_out, "dp", axis=1, tiled=True),
    )
    in_full = gathered_in[0]
    out_full = gathered_out[0]
    ff_units = in_full.shape[1] // 2
    flat_ids = expert_ids.reshape(-1)
    onehot = (flat_ids[:, None] == jnp.arange(experts, dtype=jnp.int32)[None, :]).astype(jnp.int32)
    before = jnp.cumsum(onehot, axis=0) - onehot
    position = jnp.sum(before * onehot, axis=1)
    slot_flat = flat_ids * capacity + position
    select = (
        jnp.arange(experts * capacity, dtype=jnp.int32)[:, None] == slot_flat[None, :]
    ).astype(bf16)
    diffs = router_logits[:, None, :] - router_logits[:, :, None]
    gates = 1.0 / jnp.sum(jnp.exp(diffs), axis=-1)
    upstream = cotangent.astype(f32)
    repeated = jnp.repeat(tokens, top, axis=0)
    d_picks = (gates[:, :, None] * upstream[:, None, :]).astype(bf16).reshape(-1, width)
    sendable = jnp.concatenate([repeated, d_picks], axis=1)
    outgoing = jnp.dot(select, sendable, preferred_element_type=f32).astype(bf16)
    arrived = lax.all_to_all(
        outgoing.reshape(experts, capacity, 2 * width), "expert", split_axis=0, concat_axis=0, tiled=True
    ).reshape(-1, 2 * width)
    piece = arrived[:, :width]
    d_arrived = arrived[:, width:]
    joined = jnp.dot(piece, in_full, preferred_element_type=f32)
    gate_part = joined[:, :ff_units]
    up_part = joined[:, ff_units:]
    sigma = 1.0 / (1.0 + jnp.exp(-gate_part))
    silu = gate_part * sigma
    hidden = (silu * up_part).astype(bf16)
    results = jnp.dot(hidden, out_full, preferred_element_type=f32).astype(bf16)
    returned = lax.all_to_all(
        results.reshape(experts, capacity, width), "expert", split_axis=0, concat_axis=0, tiled=True
    ).reshape(-1, width)
    d_hidden = contract_cols(d_arrived, out_full)
    grad_down = contract_rows(hidden, d_arrived)
    d_joined = jnp.concatenate(
        [d_hidden * up_part * sigma * (1.0 + gate_part * (1.0 - sigma)), d_hidden * silu], axis=1
    ).astype(bf16)
    grad_up = contract_rows(piece, d_joined)
    up_share, down_share = (
        lax.psum_scatter(grad_up.astype(bf16), "dp", scatter_dimension=0, tiled=True).astype(f32),
        lax.psum_scatter(grad_down.astype(bf16), "dp", scatter_dimension=0, tiled=True).astype(f32),
    )
    d_rows = contract_cols(d_joined, in_full).astype(bf16)
    d_back = lax.all_to_all(
        d_rows.reshape(experts, capacity, width), "expert", split_axis=0, concat_axis=0, tiled=True
    ).reshape(-1, width)
    picked = contract_rows(select, returned).reshape(tok_rows, top, width)
    mixed = jnp.einsum("tk,tkd->td", gates, picked).astype(bf16)
    d_gate = jnp.einsum("td,tkd->tk", upstream, picked)
    d_logits = gates * (d_gate - jnp.sum(gates * d_gate, axis=-1, keepdims=True))
    d_picked = contract_rows(select, d_back).reshape(tok_rows, top, width)
    d_tokens = jnp.sum(d_picked, axis=1).astype(bf16)
    return (mixed, d_tokens, d_logits, up_share[None], down_share[None])


def solution(mesh):
    placed = (
        P(("dp", "expert"), None),
        P(("dp", "expert"), None),
        P(("dp", "expert"), None),
        P(("dp", "expert"), None),
        P("expert", "dp", None),
        P("expert", "dp", None),
    )
    return jax.shard_map(
        local,
        mesh=mesh,
        in_specs=placed,
        out_specs=(
            P(("dp", "expert"), None),
            P(("dp", "expert"), None),
            P(("dp", "expert"), None),
            P("expert", "dp", None),
            P("expert", "dp", None),
        ),
        check_vma=False,
    )
```

```python
import jax
import jax.numpy as jnp
from jax import lax
from jax.sharding import PartitionSpec as P


def contract_rows(left, right):
    return lax.dot_general(
        left, right, (((0,), (0,)), ((), ())), preferred_element_type=jnp.float32
    )


def contract_cols(left, right):
    return lax.dot_general(
        left, right, (((1,), (1,)), ((), ())), preferred_element_type=jnp.float32
    )


def exchange(rows, experts, capacity, width):
    return lax.all_to_all(
        rows.reshape(experts, capacity, width), "expert", split_axis=0, concat_axis=0, tiled=True
    ).reshape(-1, width)


def body(tokens, cotangent, router_logits, expert_ids, w_in, w_out):
    f32 = jnp.float32
    bf16 = jnp.bfloat16
    tok_rows, width = tokens.shape
    top = expert_ids.shape[1]
    experts = lax.axis_size("expert")
    capacity = 7 * tok_rows * top // (4 * experts)
    gathered_in, gathered_out = (
        lax.all_gather(w_in, "dp", axis=1, tiled=True),
        lax.all_gather(w_out, "dp", axis=1, tiled=True),
    )
    in_full = gathered_in[0]
    out_full = gathered_out[0]
    ff_units = in_full.shape[1] // 2
    flat_ids = expert_ids.reshape(-1)
    onehot = (flat_ids[:, None] == jnp.arange(experts, dtype=jnp.int32)[None, :]).astype(jnp.int32)
    before = jnp.cumsum(onehot, axis=0) - onehot
    position = jnp.sum(before * onehot, axis=1)
    slot_flat = flat_ids * capacity + position
    select = (
        jnp.arange(experts * capacity, dtype=jnp.int32)[:, None] == slot_flat[None, :]
    ).astype(bf16)
    diffs = router_logits[:, None, :] - router_logits[:, :, None]
    gates = 1.0 / jnp.sum(jnp.exp(diffs), axis=-1)
    upstream = cotangent.astype(f32)
    repeated = jnp.repeat(tokens, top, axis=0)
    d_picks = (gates[:, :, None] * upstream[:, None, :]).astype(bf16).reshape(-1, width)
    sendable = jnp.concatenate([repeated, d_picks], axis=1)
    outgoing = jnp.dot(select, sendable, preferred_element_type=f32).astype(bf16)
    arrived = exchange(outgoing, experts, capacity, 2 * width)
    piece = arrived[:, :width]
    d_arrived = arrived[:, width:]
    joined = jnp.dot(piece, in_full, preferred_element_type=f32)
    gate_part = joined[:, :ff_units]
    up_part = joined[:, ff_units:]
    sigma = 1.0 / (1.0 + jnp.exp(-gate_part))
    silu = gate_part * sigma
    hidden = (silu * up_part).astype(bf16)
    results = jnp.dot(hidden, out_full, preferred_element_type=f32).astype(bf16)
    returned = exchange(results, experts, capacity, width)
    d_hidden = contract_cols(d_arrived, out_full)
    grad_down = contract_rows(hidden, d_arrived)
    d_joined = jnp.concatenate(
        [d_hidden * up_part * sigma * (1.0 + gate_part * (1.0 - sigma)), d_hidden * silu], axis=1
    ).astype(bf16)
    grad_up = contract_rows(piece, d_joined)
    d_rows = contract_cols(d_joined, in_full).astype(bf16)
    up_share, down_share = (
        lax.psum_scatter(grad_up.astype(bf16), "dp", scatter_dimension=0, tiled=True).astype(f32),
        lax.psum_scatter(grad_down.astype(bf16), "dp", scatter_dimension=0, tiled=True).astype(f32),
    )
    d_back = exchange(d_rows, experts, capacity, width)
    picked = contract_rows(select, returned).reshape(tok_rows, top, width)
    mixed = jnp.einsum("tk,tkd->td", gates, picked).astype(bf16)
    d_gate = jnp.einsum("td,tkd->tk", upstream, picked)
    d_logits = gates * (d_gate - jnp.sum(gates * d_gate, axis=-1, keepdims=True))
    d_picked = contract_rows(select, d_back).reshape(tok_rows, top, width)
    d_tokens = jnp.sum(d_picked, axis=1).astype(bf16)
    return (mixed, d_tokens, d_logits, up_share[None], down_share[None])


def solution(mesh):
    placed = (
        P(("dp", "expert"), None),
        P(("dp", "expert"), None),
        P(("dp", "expert"), None),
        P(("dp", "expert"), None),
        P("expert", "dp", None),
        P("expert", "dp", None),
    )
    return jax.shard_map(
        body,
        mesh=mesh,
        in_specs=placed,
        out_specs=(
            P(("dp", "expert"), None),
            P(("dp", "expert"), None),
            P(("dp", "expert"), None),
            P("expert", "dp", None),
            P("expert", "dp", None),
        ),
        check_vma=False,
    )
```

```python
import jax
import jax.numpy as jnp
from jax import lax
from jax.sharding import PartitionSpec as P


def contract_rows(left, right):
    return lax.dot_general(
        left, right, (((0,), (0,)), ((), ())), preferred_element_type=jnp.float32
    )


def contract_cols(left, right):
    return lax.dot_general(
        left, right, (((1,), (1,)), ((), ())), preferred_element_type=jnp.float32
    )


def exchange(rows, experts, capacity, width):
    return lax.all_to_all(
        rows.reshape(experts, capacity, width), "expert", split_axis=0, concat_axis=0, tiled=True
    ).reshape(-1, width)


def body(tokens, cotangent, router_logits, expert_ids, w_in, w_out):
    f32 = jnp.float32
    bf16 = jnp.bfloat16
    tok_rows, width = tokens.shape
    top = expert_ids.shape[1]
    experts = lax.axis_size("expert")
    capacity = 7 * tok_rows * top // (4 * experts)
    gathered_in, gathered_out = (
        lax.all_gather(w_in, "dp", axis=1, tiled=True),
        lax.all_gather(w_out, "dp", axis=1, tiled=True),
    )
    in_full = gathered_in[0]
    out_full = gathered_out[0]
    ff_units = in_full.shape[1] // 2
    flat_ids = expert_ids.reshape(-1)
    onehot = (flat_ids[:, None] == jnp.arange(experts, dtype=jnp.int32)[None, :]).astype(jnp.int32)
    before = jnp.cumsum(onehot, axis=0) - onehot
    position = jnp.sum(before * onehot, axis=1)
    slot_flat = flat_ids * capacity + position
    select = (
        jnp.arange(experts * capacity, dtype=jnp.int32)[:, None] == slot_flat[None, :]
    ).astype(bf16)
    diffs = router_logits[:, None, :] - router_logits[:, :, None]
    gates = 1.0 / jnp.sum(jnp.exp(diffs), axis=-1)
    upstream = cotangent.astype(f32)
    gates, upstream = lax.optimization_barrier((gates, upstream))
    repeated = jnp.repeat(tokens, top, axis=0)
    tok_out = jnp.dot(select, repeated, preferred_element_type=f32).astype(bf16)
    piece = exchange(tok_out, experts, capacity, width)
    d_picks = (gates[:, :, None] * upstream[:, None, :]).astype(bf16).reshape(-1, width)
    d_out = jnp.dot(select, d_picks, preferred_element_type=f32).astype(bf16)
    d_arrived = exchange(d_out, experts, capacity, width)
    joined = jnp.dot(piece, in_full, preferred_element_type=f32)
    gate_part = joined[:, :ff_units]
    up_part = joined[:, ff_units:]
    sigma = 1.0 / (1.0 + jnp.exp(-gate_part))
    silu = gate_part * sigma
    hidden = (silu * up_part).astype(bf16)
    results = jnp.dot(hidden, out_full, preferred_element_type=f32).astype(bf16)
    returned = exchange(results, experts, capacity, width)
    d_hidden = contract_cols(d_arrived, out_full)
    grad_down = contract_rows(hidden, d_arrived)
    d_joined = jnp.concatenate(
        [d_hidden * up_part * sigma * (1.0 + gate_part * (1.0 - sigma)), d_hidden * silu], axis=1
    ).astype(bf16)
    grad_up = contract_rows(piece, d_joined)
    d_rows = contract_cols(d_joined, in_full).astype(bf16)
    up_share, down_share = (
        lax.psum_scatter(grad_up.astype(bf16), "dp", scatter_dimension=0, tiled=True).astype(f32),
        lax.psum_scatter(grad_down.astype(bf16), "dp", scatter_dimension=0, tiled=True).astype(f32),
    )
    d_back = exchange(d_rows, experts, capacity, width)
    picked = contract_rows(select, returned).reshape(tok_rows, top, width)
    mixed = jnp.einsum("tk,tkd->td", gates, picked).astype(bf16)
    d_gate = jnp.einsum("td,tkd->tk", upstream, picked)
    d_logits = gates * (d_gate - jnp.sum(gates * d_gate, axis=-1, keepdims=True))
    d_picked = contract_rows(select, d_back).reshape(tok_rows, top, width)
    d_tokens = jnp.sum(d_picked, axis=1).astype(bf16)
    return (mixed, d_tokens, d_logits, up_share[None], down_share[None])


def solution(mesh):
    placed = (
        P(("dp", "expert"), None),
        P(("dp", "expert"), None),
        P(("dp", "expert"), None),
        P(("dp", "expert"), None),
        P("expert", "dp", None),
        P("expert", "dp", None),
    )
    return jax.shard_map(
        body,
        mesh=mesh,
        in_specs=placed,
        out_specs=(
            P(("dp", "expert"), None),
            P(("dp", "expert"), None),
            P(("dp", "expert"), None),
            P("expert", "dp", None),
            P("expert", "dp", None),
        ),
        check_vma=False,
    )
```

```python
import jax
import jax.numpy as jnp
from jax import lax
from jax.sharding import PartitionSpec as P


def contract_rows(left, right):
    return lax.dot_general(
        left, right, (((0,), (0,)), ((), ())), preferred_element_type=jnp.float32
    )


def contract_cols(left, right):
    return lax.dot_general(
        left, right, (((1,), (1,)), ((), ())), preferred_element_type=jnp.float32
    )


def exchange(rows, experts, capacity, width):
    lanes = 128
    return lax.all_to_all(
        rows.reshape(experts, capacity * width // lanes, lanes),
        "expert",
        split_axis=0,
        concat_axis=0,
        tiled=True,
    ).reshape(-1, width)


def body(tokens, cotangent, router_logits, expert_ids, w_in, w_out):
    f32 = jnp.float32
    bf16 = jnp.bfloat16
    tok_rows, width = tokens.shape
    top = expert_ids.shape[1]
    experts = lax.axis_size("expert")
    capacity = 7 * tok_rows * top // (4 * experts)
    gathered_in, gathered_out = (
        lax.all_gather(w_in, "dp", axis=1, tiled=True),
        lax.all_gather(w_out, "dp", axis=1, tiled=True),
    )
    in_full = gathered_in[0]
    out_full = gathered_out[0]
    ff_units = in_full.shape[1] // 2
    flat_ids = expert_ids.reshape(-1)
    onehot = (flat_ids[:, None] == jnp.arange(experts, dtype=jnp.int32)[None, :]).astype(jnp.int32)
    before = jnp.cumsum(onehot, axis=0) - onehot
    position = jnp.sum(before * onehot, axis=1)
    slot_flat = flat_ids * capacity + position
    select = (
        jnp.arange(experts * capacity, dtype=jnp.int32)[:, None] == slot_flat[None, :]
    ).astype(bf16)
    diffs = router_logits[:, None, :] - router_logits[:, :, None]
    gates = 1.0 / jnp.sum(jnp.exp(diffs), axis=-1)
    upstream = cotangent.astype(f32)
    gates, upstream = lax.optimization_barrier((gates, upstream))
    repeated = jnp.repeat(tokens, top, axis=0)
    tok_out = jnp.dot(select, repeated, preferred_element_type=f32).astype(bf16)
    piece = exchange(tok_out, experts, capacity, width)
    d_picks = (gates[:, :, None] * upstream[:, None, :]).astype(bf16).reshape(-1, width)
    d_out = jnp.dot(select, d_picks, preferred_element_type=f32).astype(bf16)
    d_arrived = exchange(d_out, experts, capacity, width)
    joined = jnp.dot(piece, in_full, preferred_element_type=f32)
    gate_part = joined[:, :ff_units]
    up_part = joined[:, ff_units:]
    sigma = 1.0 / (1.0 + jnp.exp(-gate_part))
    silu = gate_part * sigma
    hidden = (silu * up_part).astype(bf16)
    results = jnp.dot(hidden, out_full, preferred_element_type=f32).astype(bf16)
    returned = exchange(results, experts, capacity, width)
    d_hidden = contract_cols(d_arrived, out_full)
    grad_down = contract_rows(hidden, d_arrived)
    d_joined = jnp.concatenate(
        [d_hidden * up_part * sigma * (1.0 + gate_part * (1.0 - sigma)), d_hidden * silu], axis=1
    ).astype(bf16)
    grad_up = contract_rows(piece, d_joined)
    d_rows = contract_cols(d_joined, in_full).astype(bf16)
    up_share, down_share = (
        lax.psum_scatter(grad_up.astype(bf16), "dp", scatter_dimension=0, tiled=True).astype(f32),
        lax.psum_scatter(grad_down.astype(bf16), "dp", scatter_dimension=0, tiled=True).astype(f32),
    )
    d_back = exchange(d_rows, experts, capacity, width)
    picked = contract_rows(select, returned).reshape(tok_rows, top, width)
    mixed = jnp.einsum("tk,tkd->td", gates, picked).astype(bf16)
    d_gate = jnp.einsum("td,tkd->tk", upstream, picked)
    d_logits = gates * (d_gate - jnp.sum(gates * d_gate, axis=-1, keepdims=True))
    d_picked = contract_rows(select, d_back).reshape(tok_rows, top, width)
    d_tokens = jnp.sum(d_picked, axis=1).astype(bf16)
    return (mixed, d_tokens, d_logits, up_share[None], down_share[None])


def solution(mesh):
    placed = (
        P(("dp", "expert"), None),
        P(("dp", "expert"), None),
        P(("dp", "expert"), None),
        P(("dp", "expert"), None),
        P("expert", "dp", None),
        P("expert", "dp", None),
    )
    return jax.shard_map(
        body,
        mesh=mesh,
        in_specs=placed,
        out_specs=(
            P(("dp", "expert"), None),
            P(("dp", "expert"), None),
            P(("dp", "expert"), None),
            P("expert", "dp", None),
            P("expert", "dp", None),
        ),
        check_vma=False,
    )
```

```python
import jax
import jax.numpy as jnp
from jax import lax
from jax.sharding import PartitionSpec as P


def contract_rows(left, right):
    return lax.dot_general(
        left, right, (((0,), (0,)), ((), ())), preferred_element_type=jnp.float32
    )


def contract_cols(left, right):
    return lax.dot_general(
        left, right, (((1,), (1,)), ((), ())), preferred_element_type=jnp.float32
    )


def exchange(rows, experts, capacity, width):
    lanes = 128
    return lax.all_to_all(
        rows.reshape(experts, capacity * width // lanes, lanes),
        "expert",
        split_axis=0,
        concat_axis=0,
        tiled=True,
    ).reshape(-1, width)


def body(tokens, cotangent, router_logits, expert_ids, w_in, w_out):
    f32 = jnp.float32
    bf16 = jnp.bfloat16
    tok_rows, width = tokens.shape
    top = expert_ids.shape[1]
    experts = lax.axis_size("expert")
    capacity = 7 * tok_rows * top // (4 * experts)
    gathered_in, gathered_out = (
        lax.all_gather(w_in, "dp", axis=1, tiled=True),
        lax.all_gather(w_out, "dp", axis=1, tiled=True),
    )
    in_full = gathered_in[0]
    out_full = gathered_out[0]
    ff_units = in_full.shape[1] // 2
    flat_ids = expert_ids.reshape(-1)
    onehot = (flat_ids[:, None] == jnp.arange(experts, dtype=jnp.int32)[None, :]).astype(jnp.int32)
    before = jnp.cumsum(onehot, axis=0) - onehot
    position = jnp.sum(before * onehot, axis=1)
    slot_flat = flat_ids * capacity + position
    select = (
        jnp.arange(experts * capacity, dtype=jnp.int32)[:, None] == slot_flat[None, :]
    ).astype(bf16)
    diffs = router_logits[:, None, :] - router_logits[:, :, None]
    gates = 1.0 / jnp.sum(jnp.exp(diffs), axis=-1)
    upstream = cotangent.astype(f32)
    gates, upstream = lax.optimization_barrier((gates, upstream))
    repeated = jnp.repeat(tokens, top, axis=0)
    tok_out = jnp.dot(select, repeated, preferred_element_type=f32).astype(bf16)
    piece = exchange(tok_out, experts, capacity, width)
    d_picks = (gates[:, :, None] * upstream[:, None, :]).astype(bf16).reshape(-1, width)
    d_out = jnp.dot(select, d_picks, preferred_element_type=f32).astype(bf16)
    d_arrived = exchange(d_out, experts, capacity, width)
    joined = jnp.dot(piece, in_full, preferred_element_type=f32)
    gate_part = joined[:, :ff_units]
    up_part = joined[:, ff_units:]
    sigma = 1.0 / (1.0 + jnp.exp(-gate_part))
    silu = gate_part * sigma
    hidden = (silu * up_part).astype(bf16)
    results = jnp.dot(hidden, out_full, preferred_element_type=f32).astype(bf16)
    hidden, gate_part, up_part, results = lax.optimization_barrier(
        (hidden, gate_part, up_part, results)
    )
    sigma = 1.0 / (1.0 + jnp.exp(-gate_part))
    silu = gate_part * sigma
    returned = exchange(results, experts, capacity, width)
    d_hidden = contract_cols(d_arrived, out_full)
    grad_down = contract_rows(hidden, d_arrived)
    d_joined = jnp.concatenate(
        [d_hidden * up_part * sigma * (1.0 + gate_part * (1.0 - sigma)), d_hidden * silu], axis=1
    ).astype(bf16)
    grad_up = contract_rows(piece, d_joined)
    d_rows = contract_cols(d_joined, in_full).astype(bf16)
    up_share, down_share = (
        lax.psum_scatter(grad_up.astype(bf16), "dp", scatter_dimension=0, tiled=True).astype(f32),
        lax.psum_scatter(grad_down.astype(bf16), "dp", scatter_dimension=0, tiled=True).astype(f32),
    )
    d_back = exchange(d_rows, experts, capacity, width)
    picked = contract_rows(select, returned).reshape(tok_rows, top, width)
    mixed = jnp.einsum("tk,tkd->td", gates, picked).astype(bf16)
    d_gate = jnp.einsum("td,tkd->tk", upstream, picked)
    d_logits = gates * (d_gate - jnp.sum(gates * d_gate, axis=-1, keepdims=True))
    d_picked = contract_rows(select, d_back).reshape(tok_rows, top, width)
    d_tokens = jnp.sum(d_picked, axis=1).astype(bf16)
    return (mixed, d_tokens, d_logits, up_share[None], down_share[None])


def solution(mesh):
    placed = (
        P(("dp", "expert"), None),
        P(("dp", "expert"), None),
        P(("dp", "expert"), None),
        P(("dp", "expert"), None),
        P("expert", "dp", None),
        P("expert", "dp", None),
    )
    return jax.shard_map(
        body,
        mesh=mesh,
        in_specs=placed,
        out_specs=(
            P(("dp", "expert"), None),
            P(("dp", "expert"), None),
            P(("dp", "expert"), None),
            P("expert", "dp", None),
            P("expert", "dp", None),
        ),
        check_vma=False,
    )
```

```python
import jax
import jax.numpy as jnp
from jax import lax
from jax.sharding import PartitionSpec as P


def contract_rows(left, right):
    return lax.dot_general(
        left, right, (((0,), (0,)), ((), ())), preferred_element_type=jnp.float32
    )


def contract_cols(left, right):
    return lax.dot_general(
        left, right, (((1,), (1,)), ((), ())), preferred_element_type=jnp.float32
    )


def exchange(rows, experts, capacity, width):
    lanes = 128
    return lax.all_to_all(
        rows.reshape(experts, capacity * width // lanes, lanes),
        "expert",
        split_axis=0,
        concat_axis=0,
        tiled=True,
    ).reshape(-1, width)


def body(tokens, cotangent, router_logits, expert_ids, w_in, w_out):
    f32 = jnp.float32
    bf16 = jnp.bfloat16
    tok_rows, width = tokens.shape
    top = expert_ids.shape[1]
    experts = lax.axis_size("expert")
    capacity = 7 * tok_rows * top // (4 * experts)
    gathered_in, gathered_out = (
        lax.all_gather(w_in, "dp", axis=1, tiled=True),
        lax.all_gather(w_out, "dp", axis=1, tiled=True),
    )
    in_full = gathered_in[0]
    out_full = gathered_out[0]
    ff_units = in_full.shape[1] // 2
    flat_ids = expert_ids.reshape(-1)
    onehot = (flat_ids[:, None] == jnp.arange(experts, dtype=jnp.int32)[None, :]).astype(jnp.int32)
    before = jnp.cumsum(onehot, axis=0) - onehot
    position = jnp.sum(before * onehot, axis=1)
    slot_flat = flat_ids * capacity + position
    select = (
        jnp.arange(experts * capacity, dtype=jnp.int32)[:, None] == slot_flat[None, :]
    ).astype(bf16)
    diffs = router_logits[:, None, :] - router_logits[:, :, None]
    gates = 1.0 / jnp.sum(jnp.exp(diffs), axis=-1)
    upstream = cotangent.astype(f32)
    gates, upstream = lax.optimization_barrier((gates, upstream))
    token_slot = (
        jnp.arange(experts * capacity, dtype=jnp.int32)[:, None, None] == slot_flat.reshape(1, tok_rows, top)
    )
    per_token = jnp.any(token_slot, axis=2).astype(bf16)
    tok_out = jnp.dot(per_token, tokens, preferred_element_type=f32).astype(bf16)
    piece = exchange(tok_out, experts, capacity, width)
    d_picks = (gates[:, :, None] * upstream[:, None, :]).astype(bf16).reshape(-1, width)
    d_out = jnp.dot(select, d_picks, preferred_element_type=f32).astype(bf16)
    d_arrived = exchange(d_out, experts, capacity, width)
    joined = jnp.dot(piece, in_full, preferred_element_type=f32)
    gate_part = joined[:, :ff_units]
    up_part = joined[:, ff_units:]
    sigma = 1.0 / (1.0 + jnp.exp(-gate_part))
    silu = gate_part * sigma
    hidden = (silu * up_part).astype(bf16)
    results = jnp.dot(hidden, out_full, preferred_element_type=f32).astype(bf16)
    hidden, gate_part, up_part, results = lax.optimization_barrier(
        (hidden, gate_part, up_part, results)
    )
    sigma = 1.0 / (1.0 + jnp.exp(-gate_part))
    silu = gate_part * sigma
    returned = exchange(results, experts, capacity, width)
    d_hidden = contract_cols(d_arrived, out_full)
    grad_down = contract_rows(hidden, d_arrived)
    d_joined = jnp.concatenate(
        [d_hidden * up_part * sigma * (1.0 + gate_part * (1.0 - sigma)), d_hidden * silu], axis=1
    ).astype(bf16)
    grad_up = contract_rows(piece, d_joined)
    d_rows = contract_cols(d_joined, in_full).astype(bf16)
    up_part_sum, down_part_sum = (
        lax.psum_scatter(grad_up.astype(bf16), "dp", scatter_dimension=0, tiled=True),
        lax.psum_scatter(grad_down.astype(bf16), "dp", scatter_dimension=0, tiled=True),
    )
    d_back = exchange(d_rows, experts, capacity, width)
    picked = contract_rows(select, returned).reshape(tok_rows, top, width)
    mixed = jnp.einsum("tk,tkd->td", gates, picked).astype(bf16)
    d_gate = jnp.einsum("td,tkd->tk", upstream, picked)
    d_logits = gates * (d_gate - jnp.sum(gates * d_gate, axis=-1, keepdims=True))
    up_share = up_part_sum.astype(f32)
    down_share = down_part_sum.astype(f32)
    d_tokens = contract_rows(per_token, d_back).astype(bf16)
    return (mixed, d_tokens, d_logits, up_share[None], down_share[None])


def solution(mesh):
    placed = (
        P(("dp", "expert"), None),
        P(("dp", "expert"), None),
        P(("dp", "expert"), None),
        P(("dp", "expert"), None),
        P("expert", "dp", None),
        P("expert", "dp", None),
    )
    return jax.shard_map(
        body,
        mesh=mesh,
        in_specs=placed,
        out_specs=(
            P(("dp", "expert"), None),
            P(("dp", "expert"), None),
            P(("dp", "expert"), None),
            P("expert", "dp", None),
            P("expert", "dp", None),
        ),
        check_vma=False,
    )
```

```python
import jax
import jax.numpy as jnp
from jax import lax
from jax.sharding import PartitionSpec as P


def contract_rows(left, right):
    return lax.dot_general(
        left, right, (((0,), (0,)), ((), ())), preferred_element_type=jnp.float32
    )


def contract_cols(left, right):
    return lax.dot_general(
        left, right, (((1,), (1,)), ((), ())), preferred_element_type=jnp.float32
    )


def exchange(rows, experts, capacity, width):
    lanes = 128
    return lax.all_to_all(
        rows.reshape(experts, capacity * width // lanes, lanes),
        "expert",
        split_axis=0,
        concat_axis=0,
        tiled=True,
    ).reshape(-1, width)


def body(tokens, cotangent, router_logits, expert_ids, w_in, w_out):
    f32 = jnp.float32
    bf16 = jnp.bfloat16
    tok_rows, width = tokens.shape
    top = expert_ids.shape[1]
    experts = lax.axis_size("expert")
    capacity = 7 * tok_rows * top // (4 * experts)
    gathered_in, gathered_out = (
        lax.all_gather(w_in, "dp", axis=1, tiled=True),
        lax.all_gather(w_out, "dp", axis=1, tiled=True),
    )
    in_full = gathered_in[0]
    out_full = gathered_out[0]
    ff_units = in_full.shape[1] // 2
    flat_ids = expert_ids.reshape(-1)
    onehot = (flat_ids[:, None] == jnp.arange(experts, dtype=jnp.int32)[None, :]).astype(jnp.int32)
    before = jnp.cumsum(onehot, axis=0) - onehot
    position = jnp.sum(before * onehot, axis=1)
    slot_flat = flat_ids * capacity + position
    select = (
        jnp.arange(experts * capacity, dtype=jnp.int32)[:, None] == slot_flat[None, :]
    ).astype(bf16)
    diffs = router_logits[:, None, :] - router_logits[:, :, None]
    gates = 1.0 / jnp.sum(jnp.exp(diffs), axis=-1)
    upstream = cotangent.astype(f32)
    gates, upstream = lax.optimization_barrier((gates, upstream))
    token_slot = (
        jnp.arange(experts * capacity, dtype=jnp.int32)[:, None, None] == slot_flat.reshape(1, tok_rows, top)
    )
    per_token = jnp.any(token_slot, axis=2).astype(bf16)
    tok_out = jnp.dot(per_token, tokens, preferred_element_type=f32).astype(bf16)
    piece = exchange(tok_out, experts, capacity, width)
    d_picks = (gates[:, :, None] * upstream[:, None, :]).astype(bf16).reshape(-1, width)
    d_out = jnp.dot(select, d_picks, preferred_element_type=f32).astype(bf16)
    d_arrived = exchange(d_out, experts, capacity, width)
    joined = jnp.dot(piece, in_full, preferred_element_type=f32)
    gate_part = joined[:, :ff_units]
    up_part = joined[:, ff_units:]
    sigma = 1.0 / (1.0 + jnp.exp(-gate_part))
    silu = gate_part * sigma
    hidden = (silu * up_part).astype(bf16)
    results = jnp.dot(hidden, out_full, preferred_element_type=f32).astype(bf16)
    hidden, gate_part, up_part, results = lax.optimization_barrier(
        (hidden, gate_part, up_part, results)
    )
    sigma = 1.0 / (1.0 + jnp.exp(-gate_part))
    silu = gate_part * sigma
    returned = exchange(results, experts, capacity, width)
    d_hidden = contract_cols(d_arrived, out_full)
    grad_down = contract_rows(hidden, d_arrived)
    d_joined = jnp.concatenate(
        [d_hidden * up_part * sigma * (1.0 + gate_part * (1.0 - sigma)), d_hidden * silu], axis=1
    ).astype(bf16)
    grad_up = contract_rows(piece, d_joined)
    d_rows = contract_cols(d_joined, in_full).astype(bf16)
    replicas = lax.axis_size("dp")
    up_size = grad_up.size // replicas
    packed = jnp.concatenate(
        [
            grad_up.astype(bf16).reshape(replicas, up_size),
            grad_down.astype(bf16).reshape(replicas, grad_down.size // replicas),
        ],
        axis=1,
    )
    lanes = 128
    summed = lax.psum_scatter(
        packed.reshape(-1, lanes), "dp", scatter_dimension=0, tiled=True
    ).reshape(-1)
    d_back = exchange(d_rows, experts, capacity, width)
    picked = contract_rows(select, returned).reshape(tok_rows, top, width)
    mixed = jnp.einsum("tk,tkd->td", gates, picked).astype(bf16)
    d_gate = jnp.einsum("td,tkd->tk", upstream, picked)
    d_logits = gates * (d_gate - jnp.sum(gates * d_gate, axis=-1, keepdims=True))
    up_share = summed[:up_size].astype(f32).reshape(-1, grad_up.shape[1])
    down_share = summed[up_size:].astype(f32).reshape(-1, grad_down.shape[1])
    d_tokens = contract_rows(per_token, d_back).astype(bf16)
    return (mixed, d_tokens, d_logits, up_share[None], down_share[None])


def solution(mesh):
    placed = (
        P(("dp", "expert"), None),
        P(("dp", "expert"), None),
        P(("dp", "expert"), None),
        P(("dp", "expert"), None),
        P("expert", "dp", None),
        P("expert", "dp", None),
    )
    return jax.shard_map(
        body,
        mesh=mesh,
        in_specs=placed,
        out_specs=(
            P(("dp", "expert"), None),
            P(("dp", "expert"), None),
            P(("dp", "expert"), None),
            P("expert", "dp", None),
            P("expert", "dp", None),
        ),
        check_vma=False,
    )
```
